1024 devices in a mesh: dir: 32 (over z, x_hi, core), tile: 32 (over x_lo, y).
Axes of the slice: x: 8 (x_hi: 2, x_lo: 4; x = x_hi * 4 + x_lo), y: 8, z: 8, core: 2. Of those that a mesh axis runs over, the one named last changes fastest.
Arguments:
- receiver_old: float32 [64, 1024, 8, 256], P('dir', 'tile'), may hold values from -6 to 6
- receiver_now: float32 [64, 1024, 8, 256], P('dir', 'tile'), may hold values from -6 to 6
- courant: bfloat16 [64, 1024, 8, 256], P('dir', 'tile'), may hold values from 0.019897461 to 0.1796875
- source_snaps: bfloat16 [4, 64, 1024, 8, 256], P(None, 'dir', 'tile'), may hold values from -6 to 6
- recorded: bfloat16 [4, 64, 1024, 256], P(None, 'dir', 'tile'), may hold values from -6 to 6
- row_owner: int32 [64, 1024, 1], P(None, 'tile'), may hold values from 0 to 31; in each aligned block of 32 rows (0 to 31, 32 to 63, ..., all dimensions but the last counted through in order) at most 2 rows name the same one
- band_start: int32 [64, 1024], P(None, 'tile'), may hold values from 0 to 28
- band_weight: bfloat16 [64, 1024, 4], P(None, 'tile'), may hold values from 0.019897461 to 0.119628906
Outputs:
- wavefield: float32 [64, 1024, 8, 256], P('dir', 'tile')
- stack: float32 [1024, 2048], P('tile', 'dir')
The draws below stay inside these ranges and needn't reach their ends.
Inputs may be any that keep to these rules, and one draw needn't show every extreme that they name: `row_owner`: in the 32 rows of one direction held by one index of tile, no tile is named by more than 2 rows, a bound that some block reaches.
All inputs are finite; a program needn't handle non-finite values.
Results may differ from the reference program's by a relative error of at most 0.0029.
Values may be sent and summed in bfloat16 or wider, within the bound.
No kernel may reach another device: no remote copies, remote signals or barrier semaphores. Data moves between devices by JAX's collectives and lax.ppermute only.
A program may use at most 32 MiB of HBM per device.

```python
import math
import jax
import jax.numpy as jnp
import numpy as np
from jax import lax

CX = 32
NZ = 8
NY = 256
STEPS = 4
BAND = 4
DIRS = 64
NX = 1024
CAP = 2
N_TILE = 32


def place_ends(values, own_key, smallest, top_value):
    place = [jax.random.randint(jax.random.fold_in(own_key, axis), (), 0, length) for axis, length in enumerate(values.shape)]
    main_axis = values.shape.index(max(values.shape))
    neighbour = place[:main_axis] + [(place[main_axis] + 1) % values.shape[main_axis]] + place[main_axis + 1:]
    return values.at[tuple(place)].set(smallest).at[tuple(neighbour)].set(top_value)


def block_scale(rng, dims, split, least, top_value):
    loudness = 1.0
    for position, blocks in split:
        heights = jax.random.uniform(jax.random.fold_in(jax.random.fold_in(rng, 6), position), (blocks,), jnp.float32, least / len(split), top_value / len(split))
        loudness = loudness * jnp.repeat(jnp.exp(heights), dims[position] // blocks).reshape((-1,) + (1,) * (len(dims) - 1 - position))
    return loudness


def assign_block(rng, own, number, rows, count, top, bound, skew):
    ranking = jax.random.permutation(rng, count)
    crowded, ordinary = shares(count, rows * top, bound, skew, True), shares(count, rows * top, bound, skew, False)
    places = jnp.arange(count)

    def named(lengths, turn):
        used = int((lengths > 0).sum())
        fixed = max(1, used // 4)
        shifted = fixed + (places - fixed + turn * (used - fixed)) % max(1, count - fixed)
        return jnp.zeros((count,), jnp.int32).at[ranking[jnp.where(places < fixed, places, shifted)]].set(jnp.asarray(lengths, jnp.int32))

    lengths = jnp.where(number % 4 == 0, named(crowded, number // 4), named(ordinary, number - number // 4 - 1))
    mixed = jax.random.permutation(jax.random.fold_in(own, 3), count)
    giver, receiver = mixed[0:count // 2 * 2:2], mixed[1:count // 2 * 2:2]
    slack = jnp.minimum(lengths[giver] - 1, bound - lengths[receiver]) // 2
    slack = jnp.where((giver == ranking[0]) | (receiver == ranking[0]) | (lengths[receiver] == 0), 0, jnp.maximum(slack, 0))
    shifted = jax.random.randint(jax.random.fold_in(own, 4), (count // 2,), 0, 1 << 20) % (slack + 1)
    lengths = lengths.at[giver].add(-shifted).at[receiver].add(shifted)
    items = jnp.searchsorted(jnp.cumsum(lengths), jnp.arange(rows * top), side="right").astype(jnp.int32)
    listing = items.reshape(top, rows).T
    listing = listing[jax.random.permutation(jax.random.fold_in(own, 1), rows)]
    turn = jax.random.randint(jax.random.fold_in(own, 2), (rows, 1), 0, top)
    return jnp.take_along_axis(listing, (jnp.arange(top)[None, :] + turn) % top, axis=1)


def shares(number_of, total, limit, slope, full):
    loads = [(1 << 20) // math.isqrt(grade ** slope) + 1 for grade in range(1, number_of + 1)]
    largest = limit if full else min(limit, max(-(-total // number_of), total * loads[0] // sum(loads)))
    least = 1 if total - largest >= number_of - 1 else 0
    counts, surplus = [largest] + [least] * (number_of - 1), total - largest - least * (number_of - 1)
    while surplus > 0:
        free = [i for i in range(1, number_of) if counts[i] < largest] or [i for i in range(1, number_of) if counts[i] < limit]
        pool, budget = sum([loads[i] for i in free]), surplus
        for i in free:
            extra = min(limit - counts[i], max(1, budget * loads[i] // pool), surplus)
            counts[i] = counts[i] + extra
            surplus = surplus - extra
    return np.array(counts)


def normal_values(rng, extent, width, most, split=(), held_as=jnp.bfloat16):
    level = block_scale(rng, extent, split, -0.22, 0.18) if split else 1.0
    drawn = jax.random.normal(rng, extent, jnp.float32) * width * level
    return jnp.minimum(jnp.maximum(drawn, -most), most).astype(held_as)


def setup_inputs(seed: int = 0) -> dict:
    key_list = jax.random.split(jax.random.key(seed), 9)
    receiver_old = normal_values(key_list[0], (DIRS, NX, NZ, NY), 1.0, 6.0, ((0, 32), (1, 32)), jnp.float32)
    receiver_now = normal_values(key_list[1], (DIRS, NX, NZ, NY), 1.0, 6.0, ((0, 32), (1, 32)), jnp.float32)
    courant = jnp.clip(jnp.exp(math.log(0.1796875) - 2.200627 * jax.random.uniform(key_list[2], (DIRS, NX, NZ, NY), jnp.float32) ** block_scale(key_list[2], (DIRS, NX, NZ, NY), ((0, 32), (1, 32)), -0.2, 0.2)), 0.019897461, 0.1796875).astype(jnp.bfloat16)
    source_snaps = normal_values(key_list[3], (STEPS, DIRS, NX, NZ, NY), 1.0, 6.0, ((1, 32), (2, 32)))
    recorded = normal_values(key_list[4], (STEPS, DIRS, NX, NY), 1.0, 6.0, ((1, 32), (2, 32)))
    row_owner_keys = jax.random.split(jax.random.fold_in(key_list[5], 1), DIRS * NX // CX)
    row_owner_turns = jax.random.permutation(jax.random.fold_in(key_list[5], 3), DIRS * NX // CX)
    row_owner = jax.vmap(lambda own, number: assign_block(jax.random.fold_in(key_list[5], 2), own, number, CX, N_TILE, 1, CAP, 2))(row_owner_keys, row_owner_turns).reshape((DIRS, NX, 1))
    band_start = place_ends(jax.random.randint(key_list[6], (DIRS, NX), 0, CX - BAND + 1), jax.random.fold_in(key_list[6], 1), 0, CX - BAND).astype(jnp.int32)
    band_weight = jnp.clip(0.019897461 + 0.099731445 * jax.random.uniform(key_list[7], (DIRS, NX, BAND), jnp.float32) ** block_scale(key_list[7], (DIRS, NX, BAND), ((1, 32),), -0.2, 0.2), 0.019897461, 0.119628906).astype(jnp.bfloat16)
    return {"receiver_old": receiver_old, "receiver_now": receiver_now, "courant": courant, "source_snaps": source_snaps, "recorded": recorded, "row_owner": row_owner, "band_start": band_start, "band_weight": band_weight}


stencil_coef = (-205.0 / 72.0, 8.0 / 5.0, -1.0 / 5.0, 8.0 / 315.0, -1.0 / 560.0)


def laplace(padded_all, rows_here, depth, across):
    middle = padded_all[..., 4:4 + rows_here, 4:4 + depth, 4:4 + across]
    result = 3.0 * stencil_coef[0] * middle
    for reach in range(1, 5):
        plus_x = padded_all[..., 4 + reach:4 + reach + rows_here, 4:4 + depth, 4:4 + across]
        minus_x = padded_all[..., 4 - reach:4 - reach + rows_here, 4:4 + depth, 4:4 + across]
        plus_z = padded_all[..., 4:4 + rows_here, 4 + reach:4 + reach + depth, 4:4 + across]
        minus_z = padded_all[..., 4:4 + rows_here, 4 - reach:4 - reach + depth, 4:4 + across]
        plus_y = padded_all[..., 4:4 + rows_here, 4:4 + depth, 4 + reach:4 + reach + across]
        minus_y = padded_all[..., 4:4 + rows_here, 4:4 + depth, 4 - reach:4 - reach + across]
        result = result + stencil_coef[reach] * (plus_x + minus_x + plus_z + minus_z + plus_y + minus_y)
    return result


def propagate(field_old, field_now, speed, snap_set, trace_set):
    speed_wide = speed.astype(jnp.float32)
    image_sum = jnp.zeros(field_now.shape, jnp.float32)
    for step in range(STEPS):
        curvature = laplace(jnp.pad(field_now, 4), NX, NZ, NY)
        curvature = curvature.at[:, 0, :].add(trace_set[step].astype(jnp.float32))
        field_new = 2.0 * field_now - field_old + speed_wide * curvature
        image_sum = image_sum + snap_set[step].astype(jnp.float32) * field_new
        field_old, field_now = field_now, field_new
    return field_now, image_sum.astype(jnp.bfloat16).reshape(NX, NZ * NY)


def reference(receiver_old, receiver_now, courant, source_snaps, recorded, row_owner, band_start, band_weight):
    snaps = jnp.moveaxis(source_snaps, 1, 0)
    traces = jnp.moveaxis(recorded, 1, 0)

    def one_direction(stack, inputs):
        field_old, field_now, speed, snap_set, trace_set, owner_row, start_row, weight_row = inputs
        field_last, image_flat = propagate(field_old, field_now, speed, snap_set, trace_set)
        target = (owner_row[:, 0][:, None] * CX + start_row[:, None]
                  + jnp.arange(BAND, dtype=jnp.int32)[None, :]).astype(jnp.int32)
        contrib = weight_row.astype(jnp.float32)[:, :, None] * image_flat.astype(jnp.float32)[:, None, :]
        stack = stack.at[target.reshape(-1)].add(contrib.reshape(NX * BAND, NZ * NY))
        return stack, field_last

    stack, fields = lax.scan(one_direction, jnp.zeros((NX, NZ * NY), jnp.float32),
                             (receiver_old, receiver_now, courant, snaps, traces, row_owner, band_start, band_weight))
    return fields, stack
```

```python
import jax
import jax.numpy as jnp
from jax import lax
from jax.sharding import PartitionSpec as P

STEPS = 4
BAND = 4


stencil_coef = (-205.0 / 72.0, 8.0 / 5.0, -1.0 / 5.0, 8.0 / 315.0, -1.0 / 560.0)


def with_halo(value, sides, width):
    for axis, dim in sides:
        count, length = (lax.axis_size(axis), value.shape[dim])
        up = [(i, (i + 1) % count) for i in range(count - 1)]
        down = [(j, i) for i, j in up]
        last = lax.slice_in_dim(value, length - width, length, axis=dim)
        leading = lax.slice_in_dim(value, 0, width, axis=dim)
        before = lax.ppermute(last, axis, up)
        after = lax.ppermute(leading, axis, down)
        value = jnp.concatenate([before, value, after], axis=dim)
    return value


def laplace(padded_all, rows_here, depth, across):
    middle = padded_all[..., 4 : 4 + rows_here, 4 : 4 + depth, 4 : 4 + across]
    result = 3.0 * stencil_coef[0] * middle
    for reach in range(1, 5):
        plus_x = padded_all[..., 4 + reach : 4 + reach + rows_here, 4 : 4 + depth, 4 : 4 + across]
        minus_x = padded_all[..., 4 - reach : 4 - reach + rows_here, 4 : 4 + depth, 4 : 4 + across]
        plus_z = padded_all[..., 4 : 4 + rows_here, 4 + reach : 4 + reach + depth, 4 : 4 + across]
        minus_z = padded_all[..., 4 : 4 + rows_here, 4 - reach : 4 - reach + depth, 4 : 4 + across]
        plus_y = padded_all[..., 4 : 4 + rows_here, 4 : 4 + depth, 4 + reach : 4 + reach + across]
        minus_y = padded_all[..., 4 : 4 + rows_here, 4 : 4 + depth, 4 - reach : 4 - reach + across]
        result = result + stencil_coef[reach] * (
            plus_x + minus_x + plus_z + minus_z + plus_y + minus_y
        )
    return result


def band_matrix(owner, start, weight, n_tiles, n_rows):
    first = owner * n_rows + start
    place = jnp.arange(n_tiles * n_rows, dtype=jnp.int32)
    diff = place[None, None, :] - first[:, :, None]
    wide = weight.astype(jnp.bfloat16)
    zero = jnp.zeros((), jnp.bfloat16)
    out = jnp.where(diff == 0, wide[:, :, 0:1], zero)
    for k in range(1, BAND):
        out = jnp.where(diff == k, wide[:, :, k : k + 1], out)
    return out


def per_device(
    receiver_old, receiver_now, courant, source_snaps, recorded, row_owner, band_start, band_weight
):
    local_dirs, rows_here, depth, across = receiver_now.shape
    speed_wide = courant.astype(jnp.float32)
    field_old = receiver_old
    field_now = receiver_now
    image_sum = jnp.zeros(field_now.shape, jnp.float32)
    for step in range(STEPS):
        padded_x = with_halo(field_now, (("tile", 1),), 4)
        padded_all = jnp.pad(padded_x, ((0, 0), (0, 0), (4, 4), (4, 4)))
        curvature = laplace(padded_all, rows_here, depth, across)
        curvature = curvature.at[:, :, 0, :].add(recorded[step].astype(jnp.float32))
        field_new = 2.0 * field_now - field_old + speed_wide * curvature
        image_sum = image_sum + source_snaps[step].astype(jnp.float32) * field_new
        field_old, field_now = (field_now, field_new)
    image_flat = image_sum.astype(jnp.bfloat16).reshape(local_dirs, rows_here, depth * across)
    n_dir = lax.axis_size("dir")
    n_tiles = lax.axis_size("tile")
    cols = depth * across // n_dir
    blocks = image_flat.reshape(local_dirs, rows_here, n_dir, cols)
    got = lax.all_to_all(blocks, "dir", split_axis=2, concat_axis=0, tiled=True)
    all_dirs = got.shape[0]
    got = got.reshape(all_dirs * rows_here, cols)
    owner = row_owner[:, :, 0]
    mt = band_matrix(owner, band_start, band_weight, n_tiles, rows_here)
    mt = mt.reshape(all_dirs * rows_here, n_tiles * rows_here)
    partial = lax.dot_general(
        mt, got, (((0,), (0,)), ((), ())), preferred_element_type=jnp.float32
    )
    partial = partial.reshape(n_tiles, rows_here, cols)
    sent = lax.all_to_all(partial, "tile", split_axis=0, concat_axis=0, tiled=True)
    stack = jnp.sum(sent, axis=0)
    return (field_now, stack)


def solution(mesh):
    return jax.shard_map(
        per_device,
        mesh=mesh,
        in_specs=(
            P("dir", "tile", None, None),
            P("dir", "tile", None, None),
            P("dir", "tile", None, None),
            P(None, "dir", "tile", None, None),
            P(None, "dir", "tile", None),
            P(None, "tile", None),
            P(None, "tile"),
            P(None, "tile", None),
        ),
        out_specs=(P("dir", "tile", None, None), P("tile", "dir")),
        check_vma=False,
    )
```

```python
import jax
import jax.numpy as jnp
from jax import lax
from jax.sharding import PartitionSpec as P

STEPS = 4
BAND = 4


stencil_coef = (-205.0 / 72.0, 8.0 / 5.0, -1.0 / 5.0, 8.0 / 315.0, -1.0 / 560.0)


def laplace(padded_all, rows_here, depth, across):
    middle = padded_all[..., 4 : 4 + rows_here, 4 : 4 + depth, 4 : 4 + across]
    result = 3.0 * stencil_coef[0] * middle
    for reach in range(1, 5):
        plus_x = padded_all[..., 4 + reach : 4 + reach + rows_here, 4 : 4 + depth, 4 : 4 + across]
        minus_x = padded_all[..., 4 - reach : 4 - reach + rows_here, 4 : 4 + depth, 4 : 4 + across]
        plus_z = padded_all[..., 4 : 4 + rows_here, 4 + reach : 4 + reach + depth, 4 : 4 + across]
        minus_z = padded_all[..., 4 : 4 + rows_here, 4 - reach : 4 - reach + depth, 4 : 4 + across]
        plus_y = padded_all[..., 4 : 4 + rows_here, 4 : 4 + depth, 4 + reach : 4 + reach + across]
        minus_y = padded_all[..., 4 : 4 + rows_here, 4 : 4 + depth, 4 - reach : 4 - reach + across]
        result = result + stencil_coef[reach] * (
            plus_x + minus_x + plus_z + minus_z + plus_y + minus_y
        )
    return result


def band_matrix(owner, start, weight, n_tiles, n_rows):
    first = owner * n_rows + start
    place = jnp.arange(n_tiles * n_rows, dtype=jnp.int32)
    diff = place[None, None, :] - first[:, :, None]
    wide = weight.astype(jnp.bfloat16)
    zero = jnp.zeros((), jnp.bfloat16)
    out = jnp.where(diff == 0, wide[:, :, 0:1], zero)
    for k in range(1, BAND):
        out = jnp.where(diff == k, wide[:, :, k : k + 1], out)
    return out


def exchange_halo(parts):
    count = lax.axis_size("tile")
    up = [(i, i + 1) for i in range(count - 1)]
    down = [(j, i) for i, j in up]
    tails = jnp.concatenate([lax.slice_in_dim(p, p.shape[d] - w, p.shape[d], axis=d).reshape(-1) for p, d, w in parts])
    heads = jnp.concatenate([lax.slice_in_dim(p, 0, w, axis=d).reshape(-1) for p, d, w in parts])
    before = lax.ppermute(tails, "tile", up)
    after = lax.ppermute(heads, "tile", down)
    return before, after


def unpack(flat, parts):
    out = []
    offset = 0
    for p, d, w in parts:
        shape = list(p.shape)
        shape[d] = w
        size = 1
        for n in shape:
            size *= n
        out.append(flat[offset : offset + size].reshape(shape))
        offset += size
    return out


def per_device(
    receiver_old, receiver_now, courant, source_snaps, recorded, row_owner, band_start, band_weight
):
    local_dirs, rows_here, depth, across = receiver_now.shape
    reach = 4
    halo = reach * STEPS
    wide_parts = [(receiver_now, 1, halo), (receiver_old, 1, halo - reach)]
    narrow_parts = [(courant, 1, halo - reach), (recorded, 2, halo - reach)]
    wide_before, wide_after = exchange_halo(wide_parts)
    narrow_before, narrow_after = exchange_halo(narrow_parts)
    now_b, old_b = unpack(wide_before, wide_parts)
    now_a, old_a = unpack(wide_after, wide_parts)
    c_b, rec_b = unpack(narrow_before, narrow_parts)
    c_a, rec_a = unpack(narrow_after, narrow_parts)
    field_now = jnp.concatenate([now_b, receiver_now, now_a], axis=1)
    field_old = jnp.concatenate([old_b, receiver_old, old_a], axis=1)
    speed_wide = jnp.concatenate([c_b, courant, c_a], axis=1).astype(jnp.float32)
    rec_wide = jnp.concatenate([rec_b, recorded, rec_a], axis=2).astype(jnp.float32)
    plane = lax.broadcasted_iota(jnp.int32, (1, 1, depth, 1), 2)
    image_sum = jnp.zeros(receiver_now.shape, jnp.float32)
    for step in range(STEPS):
        ext_in = halo - reach * step
        ext_out = ext_in - reach
        rows_out = rows_here + 2 * ext_out
        lo = (halo - reach) - ext_out
        padded_all = jnp.pad(field_now, ((0, 0), (0, 0), (4, 4), (4, 4)))
        curvature = laplace(padded_all, rows_out, depth, across)
        inject = rec_wide[step][:, lo : lo + rows_out, None, :]
        curvature = curvature + jnp.where(plane == 0, inject, 0.0)
        now_mid = field_now[:, reach : reach + rows_out]
        old_off = field_old.shape[1] // 2 - rows_out // 2
        old_mid = field_old[:, old_off : old_off + rows_out]
        speed_mid = speed_wide[:, lo : lo + rows_out]
        field_new = 2.0 * now_mid - old_mid + speed_mid * curvature
        image_sum = image_sum + source_snaps[step].astype(jnp.float32) * field_new[
            :, ext_out : ext_out + rows_here
        ]
        field_old, field_now = (field_now, field_new)
    image_flat = image_sum.astype(jnp.bfloat16).reshape(local_dirs, rows_here, depth * across)
    n_dir = lax.axis_size("dir")
    n_tiles = lax.axis_size("tile")
    cols = depth * across // n_dir
    blocks = image_flat.reshape(local_dirs, rows_here, n_dir, cols)
    got = lax.all_to_all(blocks, "dir", split_axis=2, concat_axis=0, tiled=True)
    all_dirs = got.shape[0]
    got = got.reshape(all_dirs * rows_here, cols)
    owner = row_owner[:, :, 0]
    mt = band_matrix(owner, band_start, band_weight, n_tiles, rows_here)
    mt = mt.reshape(all_dirs * rows_here, n_tiles * rows_here)
    partial = lax.dot_general(
        mt, got, (((0,), (0,)), ((), ())), preferred_element_type=jnp.float32
    )
    partial = partial.reshape(n_tiles, rows_here, cols)
    sent = lax.all_to_all(partial, "tile", split_axis=0, concat_axis=0, tiled=True)
    stack = jnp.sum(sent, axis=0)
    return (field_now, stack)


def solution(mesh):
    return jax.shard_map(
        per_device,
        mesh=mesh,
        in_specs=(
            P("dir", "tile", None, None),
            P("dir", "tile", None, None),
            P("dir", "tile", None, None),
            P(None, "dir", "tile", None, None),
            P(None, "dir", "tile", None),
            P(None, "tile", None),
            P(None, "tile"),
            P(None, "tile", None),
        ),
        out_specs=(P("dir", "tile", None, None), P("tile", "dir")),
        check_vma=False,
    )
```

```python
import jax
import jax.numpy as jnp
from jax import lax
from jax.sharding import PartitionSpec as P

STEPS = 4
BAND = 4


stencil_coef = (-205.0 / 72.0, 8.0 / 5.0, -1.0 / 5.0, 8.0 / 315.0, -1.0 / 560.0)


def laplace(padded_all, rows_here, depth, across):
    middle = padded_all[..., 4 : 4 + rows_here, 4 : 4 + depth, 4 : 4 + across]
    result = 3.0 * stencil_coef[0] * middle
    for reach in range(1, 5):
        plus_x = padded_all[..., 4 + reach : 4 + reach + rows_here, 4 : 4 + depth, 4 : 4 + across]
        minus_x = padded_all[..., 4 - reach : 4 - reach + rows_here, 4 : 4 + depth, 4 : 4 + across]
        plus_z = padded_all[..., 4 : 4 + rows_here, 4 + reach : 4 + reach + depth, 4 : 4 + across]
        minus_z = padded_all[..., 4 : 4 + rows_here, 4 - reach : 4 - reach + depth, 4 : 4 + across]
        plus_y = padded_all[..., 4 : 4 + rows_here, 4 : 4 + depth, 4 + reach : 4 + reach + across]
        minus_y = padded_all[..., 4 : 4 + rows_here, 4 : 4 + depth, 4 - reach : 4 - reach + across]
        result = result + stencil_coef[reach] * (
            plus_x + minus_x + plus_z + minus_z + plus_y + minus_y
        )
    return result


def band_matrix(owner, start, weight, n_tiles, n_rows):
    first = owner * n_rows + start
    place = jnp.arange(n_tiles * n_rows, dtype=jnp.int32)
    diff = place[None, None, :] - first[:, :, None]
    wide = weight.astype(jnp.bfloat16)
    zero = jnp.zeros((), jnp.bfloat16)
    out = jnp.where(diff == 0, wide[:, :, 0:1], zero)
    for k in range(1, BAND):
        out = jnp.where(diff == k, wide[:, :, k : k + 1], out)
    return out


def exchange_halo(tails, heads):
    count = lax.axis_size("tile")
    up = [(i, i + 1) for i in range(count - 1)]
    down = [(j, i) for i, j in up]
    return lax.ppermute(tails, "tile", up), lax.ppermute(heads, "tile", down)


def per_device(
    receiver_old, receiver_now, courant, source_snaps, recorded, row_owner, band_start, band_weight
):
    local_dirs, rows_here, depth, across = receiver_now.shape
    reach = 4
    halo = reach * STEPS
    old_halo = halo - reach
    wide_before, wide_after = exchange_halo(
        jnp.concatenate([receiver_now[:, -halo:], receiver_old[:, -old_halo:]], axis=1),
        jnp.concatenate([receiver_now[:, :halo], receiver_old[:, :old_halo]], axis=1),
    )
    traces = jnp.moveaxis(recorded, 0, 2)
    narrow_before, narrow_after = exchange_halo(
        jnp.concatenate([courant[:, -old_halo:], traces[:, -old_halo:]], axis=2),
        jnp.concatenate([courant[:, :old_halo], traces[:, :old_halo]], axis=2),
    )
    now_b, old_b = wide_before[:, :halo], wide_before[:, halo:]
    now_a, old_a = wide_after[:, :halo], wide_after[:, halo:]
    c_b, rec_b = narrow_before[:, :, :depth], jnp.moveaxis(narrow_before[:, :, depth:], 2, 0)
    c_a, rec_a = narrow_after[:, :, :depth], jnp.moveaxis(narrow_after[:, :, depth:], 2, 0)
    field_now = jnp.concatenate([now_b, receiver_now, now_a], axis=1)
    field_old = jnp.concatenate([old_b, receiver_old, old_a], axis=1)
    speed_wide = jnp.concatenate([c_b, courant, c_a], axis=1).astype(jnp.float32)
    rec_wide = jnp.concatenate([rec_b, recorded, rec_a], axis=2).astype(jnp.float32)
    plane = lax.broadcasted_iota(jnp.int32, (1, 1, depth, 1), 2)
    image_sum = jnp.zeros(receiver_now.shape, jnp.float32)
    for step in range(STEPS):
        ext_in = halo - reach * step
        ext_out = ext_in - reach
        rows_out = rows_here + 2 * ext_out
        lo = (halo - reach) - ext_out
        padded_all = jnp.pad(field_now, ((0, 0), (0, 0), (4, 4), (4, 4)))
        curvature = laplace(padded_all, rows_out, depth, across)
        inject = rec_wide[step][:, lo : lo + rows_out, None, :]
        curvature = curvature + jnp.where(plane == 0, inject, 0.0)
        now_mid = field_now[:, reach : reach + rows_out]
        old_off = field_old.shape[1] // 2 - rows_out // 2
        old_mid = field_old[:, old_off : old_off + rows_out]
        speed_mid = speed_wide[:, lo : lo + rows_out]
        field_new = 2.0 * now_mid - old_mid + speed_mid * curvature
        image_sum = image_sum + source_snaps[step].astype(jnp.float32) * field_new[
            :, ext_out : ext_out + rows_here
        ]
        field_old, field_now = (field_now, field_new)
    image_flat = image_sum.astype(jnp.bfloat16).reshape(local_dirs, rows_here, depth * across)
    n_dir = lax.axis_size("dir")
    n_tiles = lax.axis_size("tile")
    cols = depth * across // n_dir
    blocks = image_flat.reshape(local_dirs, rows_here, n_dir, cols)
    got = lax.all_to_all(blocks, "dir", split_axis=2, concat_axis=0, tiled=True)
    all_dirs = got.shape[0]
    got = got.reshape(all_dirs * rows_here, cols)
    owner = row_owner[:, :, 0]
    mt = band_matrix(owner, band_start, band_weight, n_tiles, rows_here)
    mt = mt.reshape(all_dirs * rows_here, n_tiles * rows_here)
    partial = lax.dot_general(
        mt, got, (((0,), (0,)), ((), ())), preferred_element_type=jnp.float32
    )
    partial = partial.reshape(n_tiles, rows_here, cols)
    sent = lax.all_to_all(partial, "tile", split_axis=0, concat_axis=0, tiled=True)
    stack = jnp.sum(sent, axis=0)
    return (field_now, stack)


def solution(mesh):
    return jax.shard_map(
        per_device,
        mesh=mesh,
        in_specs=(
            P("dir", "tile", None, None),
            P("dir", "tile", None, None),
            P("dir", "tile", None, None),
            P(None, "dir", "tile", None, None),
            P(None, "dir", "tile", None),
            P(None, "tile", None),
            P(None, "tile"),
            P(None, "tile", None),
        ),
        out_specs=(P("dir", "tile", None, None), P("tile", "dir")),
        check_vma=False,
    )
```

```python
import jax
import jax.numpy as jnp
from jax import lax
from jax.sharding import PartitionSpec as P

STEPS = 4
BAND = 4


stencil_coef = (-205.0 / 72.0, 8.0 / 5.0, -1.0 / 5.0, 8.0 / 315.0, -1.0 / 560.0)


def laplace(padded_all, rows_here, depth, across):
    middle = padded_all[..., 4 : 4 + rows_here, 4 : 4 + depth, 4 : 4 + across]
    result = 3.0 * stencil_coef[0] * middle
    for reach in range(1, 5):
        plus_x = padded_all[..., 4 + reach : 4 + reach + rows_here, 4 : 4 + depth, 4 : 4 + across]
        minus_x = padded_all[..., 4 - reach : 4 - reach + rows_here, 4 : 4 + depth, 4 : 4 + across]
        plus_z = padded_all[..., 4 : 4 + rows_here, 4 + reach : 4 + reach + depth, 4 : 4 + across]
        minus_z = padded_all[..., 4 : 4 + rows_here, 4 - reach : 4 - reach + depth, 4 : 4 + across]
        plus_y = padded_all[..., 4 : 4 + rows_here, 4 : 4 + depth, 4 + reach : 4 + reach + across]
        minus_y = padded_all[..., 4 : 4 + rows_here, 4 : 4 + depth, 4 - reach : 4 - reach + across]
        result = result + stencil_coef[reach] * (
            plus_x + minus_x + plus_z + minus_z + plus_y + minus_y
        )
    return result


def band_matrix(owner, start, weight, n_tiles, n_rows):
    first = owner * n_rows + start
    place = jnp.arange(n_tiles * n_rows, dtype=jnp.int32)
    diff = place[None, None, :] - first[:, :, None]
    wide = weight.astype(jnp.bfloat16)
    zero = jnp.zeros((), jnp.bfloat16)
    out = jnp.where(diff == 0, wide[:, :, 0:1], zero)
    for k in range(1, BAND):
        out = jnp.where(diff == k, wide[:, :, k : k + 1], out)
    return out


def exchange_halo(tails, heads):
    count = lax.axis_size("tile")
    up = [(i, i + 1) for i in range(count - 1)]
    down = [(j, i) for i, j in up]
    return lax.ppermute(tails, "tile", up), lax.ppermute(heads, "tile", down)


def per_device(
    receiver_old, receiver_now, courant, source_snaps, recorded, row_owner, band_start, band_weight
):
    local_dirs, rows_here, depth, across = receiver_now.shape
    reach = 4
    halo = reach * STEPS
    old_halo = halo - reach
    wide_before, wide_after = exchange_halo(
        jnp.concatenate([receiver_now[:, -halo:], receiver_old[:, -old_halo:]], axis=1),
        jnp.concatenate([receiver_now[:, :halo], receiver_old[:, :old_halo]], axis=1),
    )
    traces = jnp.moveaxis(recorded, 0, 2)
    narrow_before, narrow_after = exchange_halo(
        jnp.concatenate([courant[:, -old_halo:], traces[:, -old_halo:]], axis=2),
        jnp.concatenate([courant[:, :old_halo], traces[:, :old_halo]], axis=2),
    )
    now_b, old_b = wide_before[:, :halo], wide_before[:, halo:]
    now_a, old_a = wide_after[:, :halo], wide_after[:, halo:]
    c_b, rec_b = narrow_before[:, :, :depth], jnp.moveaxis(narrow_before[:, :, depth:], 2, 0)
    c_a, rec_a = narrow_after[:, :, :depth], jnp.moveaxis(narrow_after[:, :, depth:], 2, 0)
    field_now = jnp.concatenate([now_b, receiver_now, now_a], axis=1)
    field_old = jnp.concatenate([old_b, receiver_old, old_a], axis=1)
    speed_wide = jnp.concatenate([c_b, courant, c_a], axis=1).astype(jnp.float32)
    rec_wide = jnp.concatenate([rec_b, recorded, rec_a], axis=2).astype(jnp.float32)
    plane = lax.broadcasted_iota(jnp.int32, (1, 1, depth, 1), 2)
    image_sum = jnp.zeros(receiver_now.shape, jnp.float32)
    for step in range(STEPS):
        ext_in = halo - reach * step
        ext_out = ext_in - reach
        rows_out = rows_here + 2 * ext_out
        lo = (halo - reach) - ext_out
        padded_all = jnp.pad(field_now, ((0, 0), (0, 0), (4, 4), (4, 4)))
        curvature = laplace(padded_all, rows_out, depth, across)
        inject = rec_wide[step][:, lo : lo + rows_out, None, :]
        curvature = curvature + jnp.where(plane == 0, inject, 0.0)
        now_mid = field_now[:, reach : reach + rows_out]
        old_off = field_old.shape[1] // 2 - rows_out // 2
        old_mid = field_old[:, old_off : old_off + rows_out]
        speed_mid = speed_wide[:, lo : lo + rows_out]
        field_new = 2.0 * now_mid - old_mid + speed_mid * curvature
        image_sum = image_sum + source_snaps[step].astype(jnp.float32) * field_new[
            :, ext_out : ext_out + rows_here
        ]
        field_old, field_now = (field_now, field_new)
    image_flat = image_sum.astype(jnp.bfloat16).reshape(local_dirs, rows_here, depth * across)
    n_dir = lax.axis_size("dir")
    n_tiles = lax.axis_size("tile")
    cols = depth * across // n_dir
    blocks = image_flat.reshape(local_dirs, rows_here, n_dir, cols)
    got = lax.all_to_all(blocks, "dir", split_axis=2, concat_axis=0, tiled=True)
    all_dirs = got.shape[0]
    got = got.reshape(all_dirs * rows_here, cols)
    owner = row_owner[:, :, 0]
    mt = band_matrix(owner, band_start, band_weight, n_tiles, rows_here)
    mt = lax.optimization_barrier(mt.reshape(all_dirs * rows_here, n_tiles * rows_here))
    partial = lax.dot_general(
        mt, got, (((0,), (0,)), ((), ())), preferred_element_type=jnp.float32
    )
    partial = partial.reshape(n_tiles, rows_here * cols)
    sent = lax.all_to_all(partial, "tile", split_axis=0, concat_axis=0, tiled=True)
    stack = jnp.sum(sent.reshape(n_tiles, rows_here, cols), axis=0)
    return (field_now, stack)


def solution(mesh):
    return jax.shard_map(
        per_device,
        mesh=mesh,
        in_specs=(
            P("dir", "tile", None, None),
            P("dir", "tile", None, None),
            P("dir", "tile", None, None),
            P(None, "dir", "tile", None, None),
            P(None, "dir", "tile", None),
            P(None, "tile", None),
            P(None, "tile"),
            P(None, "tile", None),
        ),
        out_specs=(P("dir", "tile", None, None), P("tile", "dir")),
        check_vma=False,
    )
```

```python
import jax
import jax.numpy as jnp
from jax import lax
from jax.sharding import PartitionSpec as P

STEPS = 4
BAND = 4


stencil_coef = (-205.0 / 72.0, 8.0 / 5.0, -1.0 / 5.0, 8.0 / 315.0, -1.0 / 560.0)


def laplace(padded_all, rows_here, depth, across):
    middle = padded_all[..., 4 : 4 + rows_here, 4 : 4 + depth, 4 : 4 + across]
    result = 3.0 * stencil_coef[0] * middle
    for reach in range(1, 5):
        plus_x = padded_all[..., 4 + reach : 4 + reach + rows_here, 4 : 4 + depth, 4 : 4 + across]
        minus_x = padded_all[..., 4 - reach : 4 - reach + rows_here, 4 : 4 + depth, 4 : 4 + across]
        plus_z = padded_all[..., 4 : 4 + rows_here, 4 + reach : 4 + reach + depth, 4 : 4 + across]
        minus_z = padded_all[..., 4 : 4 + rows_here, 4 - reach : 4 - reach + depth, 4 : 4 + across]
        plus_y = padded_all[..., 4 : 4 + rows_here, 4 : 4 + depth, 4 + reach : 4 + reach + across]
        minus_y = padded_all[..., 4 : 4 + rows_here, 4 : 4 + depth, 4 - reach : 4 - reach + across]
        result = result + stencil_coef[reach] * (
            plus_x + minus_x + plus_z + minus_z + plus_y + minus_y
        )
    return result


def band_matrix(owner, start, weight, n_tiles, n_rows):
    first = owner * n_rows + start
    place = jnp.arange(n_tiles * n_rows, dtype=jnp.int32)
    diff = place[None, None, :] - first[:, :, None]
    wide = weight.astype(jnp.bfloat16)
    zero = jnp.zeros((), jnp.bfloat16)
    out = jnp.where(diff == 0, wide[:, :, 0:1], zero)
    for k in range(1, BAND):
        out = jnp.where(diff == k, wide[:, :, k : k + 1], out)
    return out


def exchange_halo(tails, heads):
    count = lax.axis_size("tile")
    up = [(i, i + 1) for i in range(count - 1)]
    down = [(j, i) for i, j in up]
    return lax.ppermute(tails, "tile", up), lax.ppermute(heads, "tile", down)


def per_device(
    receiver_old, receiver_now, courant, source_snaps, recorded, row_owner, band_start, band_weight
):
    local_dirs, rows_here, depth, across = receiver_now.shape
    reach = 4
    halo = reach * STEPS
    old_halo = halo - reach
    wide_before, wide_after = exchange_halo(
        jnp.concatenate([receiver_now[:, -halo:], receiver_old[:, -old_halo:]], axis=1),
        jnp.concatenate([receiver_now[:, :halo], receiver_old[:, :old_halo]], axis=1),
    )
    traces = jnp.moveaxis(recorded, 0, 2)
    narrow_before, narrow_after = exchange_halo(
        jnp.concatenate([courant[:, -old_halo:], traces[:, -old_halo:]], axis=2),
        jnp.concatenate([courant[:, :old_halo], traces[:, :old_halo]], axis=2),
    )
    now_b, old_b = wide_before[:, :halo], wide_before[:, halo:]
    now_a, old_a = wide_after[:, :halo], wide_after[:, halo:]
    c_b, rec_b = narrow_before[:, :, :depth], jnp.moveaxis(narrow_before[:, :, depth:], 2, 0)
    c_a, rec_a = narrow_after[:, :, :depth], jnp.moveaxis(narrow_after[:, :, depth:], 2, 0)
    field_now = jnp.concatenate([now_b, receiver_now, now_a], axis=1)
    field_old = jnp.concatenate([old_b, receiver_old, old_a], axis=1)
    speed_wide = jnp.concatenate([c_b, courant, c_a], axis=1).astype(jnp.float32)
    rec_wide = jnp.concatenate([rec_b, recorded, rec_a], axis=2).astype(jnp.float32)
    plane = lax.broadcasted_iota(jnp.int32, (1, 1, depth, 1), 2)
    image_sum = jnp.zeros(receiver_now.shape, jnp.float32)
    for step in range(STEPS):
        ext_in = halo - reach * step
        ext_out = ext_in - reach
        rows_out = rows_here + 2 * ext_out
        lo = (halo - reach) - ext_out
        padded_all = jnp.pad(field_now, ((0, 0), (0, 0), (4, 4), (4, 4)))
        curvature = laplace(padded_all, rows_out, depth, across)
        inject = rec_wide[step][:, lo : lo + rows_out, None, :]
        curvature = curvature + jnp.where(plane == 0, inject, 0.0)
        now_mid = field_now[:, reach : reach + rows_out]
        old_off = field_old.shape[1] // 2 - rows_out // 2
        old_mid = field_old[:, old_off : old_off + rows_out]
        speed_mid = speed_wide[:, lo : lo + rows_out]
        field_new = 2.0 * now_mid - old_mid + speed_mid * curvature
        image_sum = image_sum + source_snaps[step].astype(jnp.float32) * field_new[
            :, ext_out : ext_out + rows_here
        ]
        field_old, field_now = (field_now, field_new)
    image_flat = image_sum.astype(jnp.bfloat16).reshape(local_dirs, rows_here, depth * across)
    n_dir = lax.axis_size("dir")
    n_tiles = lax.axis_size("tile")
    cols = depth * across // n_dir
    blocks = image_flat.reshape(local_dirs, rows_here, n_dir, cols)
    got = lax.all_to_all(blocks, "dir", split_axis=2, concat_axis=0, tiled=True)
    all_dirs = got.shape[0]
    got = got.reshape(all_dirs * rows_here, cols)
    owner = row_owner[:, :, 0]
    mt = band_matrix(owner, band_start, band_weight, n_tiles, rows_here)
    mt = mt.reshape(all_dirs * rows_here, n_tiles * rows_here)
    partial = lax.dot_general(
        mt, got, (((0,), (0,)), ((), ())), preferred_element_type=jnp.float32
    )
    partial = partial.reshape(n_tiles, rows_here * cols)
    sent = lax.all_to_all(partial, "tile", split_axis=0, concat_axis=0, tiled=True)
    stack = jnp.sum(sent.reshape(n_tiles, rows_here, cols), axis=0)
    return (field_now, stack)


def solution(mesh):
    return jax.shard_map(
        per_device,
        mesh=mesh,
        in_specs=(
            P("dir", "tile", None, None),
            P("dir", "tile", None, None),
            P("dir", "tile", None, None),
            P(None, "dir", "tile", None, None),
            P(None, "dir", "tile", None),
            P(None, "tile", None),
            P(None, "tile"),
            P(None, "tile", None),
        ),
        out_specs=(P("dir", "tile", None, None), P("tile", "dir")),
        check_vma=False,
    )
```

```python
import jax
import jax.numpy as jnp
from jax import lax
from jax.sharding import PartitionSpec as P

STEPS = 4
BAND = 4


stencil_coef = (-205.0 / 72.0, 8.0 / 5.0, -1.0 / 5.0, 8.0 / 315.0, -1.0 / 560.0)


def laplace(padded_all, rows_here, depth, across):
    middle = padded_all[..., 4 : 4 + rows_here, 4 : 4 + depth, 4 : 4 + across]
    result = 3.0 * stencil_coef[0] * middle
    for reach in range(1, 5):
        plus_x = padded_all[..., 4 + reach : 4 + reach + rows_here, 4 : 4 + depth, 4 : 4 + across]
        minus_x = padded_all[..., 4 - reach : 4 - reach + rows_here, 4 : 4 + depth, 4 : 4 + across]
        plus_z = padded_all[..., 4 : 4 + rows_here, 4 + reach : 4 + reach + depth, 4 : 4 + across]
        minus_z = padded_all[..., 4 : 4 + rows_here, 4 - reach : 4 - reach + depth, 4 : 4 + across]
        plus_y = padded_all[..., 4 : 4 + rows_here, 4 : 4 + depth, 4 + reach : 4 + reach + across]
        minus_y = padded_all[..., 4 : 4 + rows_here, 4 : 4 + depth, 4 - reach : 4 - reach + across]
        result = result + stencil_coef[reach] * (
            plus_x + minus_x + plus_z + minus_z + plus_y + minus_y
        )
    return result


def band_matrix(owner, start, weight, n_tiles, n_rows):
    first = owner * n_rows + start
    place = jnp.arange(n_tiles * n_rows, dtype=jnp.int32)
    diff = place[None, None, :] - first[:, :, None]
    wide = weight.astype(jnp.bfloat16)
    zero = jnp.zeros((), jnp.bfloat16)
    out = jnp.where(diff == 0, wide[:, :, 0:1], zero)
    for k in range(1, BAND):
        out = jnp.where(diff == k, wide[:, :, k : k + 1], out)
    return out


def exchange_halo(tails, heads):
    count = lax.axis_size("tile")
    up = [(i, i + 1) for i in range(count - 1)]
    down = [(j, i) for i, j in up]
    return lax.ppermute(tails, "tile", up), lax.ppermute(heads, "tile", down)


def per_device(
    receiver_old, receiver_now, courant, source_snaps, recorded, row_owner, band_start, band_weight
):
    local_dirs, rows_here, depth, across = receiver_now.shape
    reach = 4
    halo = reach * STEPS
    old_halo = halo - reach
    traces = jnp.pad(jnp.moveaxis(recorded, 0, 2), ((0, 0), (0, 0), (0, depth - STEPS), (0, 0)))
    last_static = jnp.concatenate([courant[:, -old_halo:], traces[:, -old_halo:]], axis=1)
    first_static = jnp.concatenate([courant[:, :old_halo], traces[:, :old_halo]], axis=1)
    before, after = exchange_halo(
        jnp.concatenate(
            [receiver_now[:, -halo:], receiver_old[:, -old_halo:], last_static.astype(jnp.float32)], axis=1
        ),
        jnp.concatenate(
            [receiver_now[:, :halo], receiver_old[:, :old_halo], first_static.astype(jnp.float32)], axis=1
        ),
    )
    edges = (halo, halo + old_halo, halo + 2 * old_halo)
    now_b, old_b, c_b, rec_b = jnp.split(before, edges, axis=1)
    now_a, old_a, c_a, rec_a = jnp.split(after, edges, axis=1)
    field_now = jnp.concatenate([now_b, receiver_now, now_a], axis=1)
    field_old = jnp.concatenate([old_b, receiver_old, old_a], axis=1)
    speed_wide = jnp.concatenate([c_b, courant.astype(jnp.float32), c_a], axis=1)
    rec_wide = jnp.concatenate([rec_b, traces.astype(jnp.float32), rec_a], axis=1)
    rec_wide = jnp.moveaxis(rec_wide[:, :, :STEPS], 2, 0)
    plane = lax.broadcasted_iota(jnp.int32, (1, 1, depth, 1), 2)
    image_sum = jnp.zeros(receiver_now.shape, jnp.float32)
    for step in range(STEPS):
        ext_in = halo - reach * step
        ext_out = ext_in - reach
        rows_out = rows_here + 2 * ext_out
        lo = (halo - reach) - ext_out
        padded_all = jnp.pad(field_now, ((0, 0), (0, 0), (4, 4), (4, 4)))
        curvature = laplace(padded_all, rows_out, depth, across)
        inject = rec_wide[step][:, lo : lo + rows_out, None, :]
        curvature = curvature + jnp.where(plane == 0, inject, 0.0)
        now_mid = field_now[:, reach : reach + rows_out]
        old_off = field_old.shape[1] // 2 - rows_out // 2
        old_mid = field_old[:, old_off : old_off + rows_out]
        speed_mid = speed_wide[:, lo : lo + rows_out]
        field_new = 2.0 * now_mid - old_mid + speed_mid * curvature
        image_sum = image_sum + source_snaps[step].astype(jnp.float32) * field_new[
            :, ext_out : ext_out + rows_here
        ]
        field_old, field_now = (field_now, field_new)
    image_flat = image_sum.astype(jnp.bfloat16).reshape(local_dirs, rows_here, depth * across)
    n_dir = lax.axis_size("dir")
    n_tiles = lax.axis_size("tile")
    cols = depth * across // n_dir
    blocks = image_flat.reshape(local_dirs, rows_here, n_dir, cols)
    got = lax.all_to_all(blocks, "dir", split_axis=2, concat_axis=0, tiled=True)
    all_dirs = got.shape[0]
    got = got.reshape(all_dirs * rows_here, cols)
    owner = row_owner[:, :, 0]
    mt = band_matrix(owner, band_start, band_weight, n_tiles, rows_here)
    mt = mt.reshape(all_dirs * rows_here, n_tiles * rows_here)
    partial = lax.dot_general(
        mt, got, (((0,), (0,)), ((), ())), preferred_element_type=jnp.float32
    )
    partial = partial.reshape(n_tiles, rows_here * cols)
    sent = lax.all_to_all(partial, "tile", split_axis=0, concat_axis=0, tiled=True)
    stack = jnp.sum(sent.reshape(n_tiles, rows_here, cols), axis=0)
    return (field_now, stack)


def solution(mesh):
    return jax.shard_map(
        per_device,
        mesh=mesh,
        in_specs=(
            P("dir", "tile", None, None),
            P("dir", "tile", None, None),
            P("dir", "tile", None, None),
            P(None, "dir", "tile", None, None),
            P(None, "dir", "tile", None),
            P(None, "tile", None),
            P(None, "tile"),
            P(None, "tile", None),
        ),
        out_specs=(P("dir", "tile", None, None), P("tile", "dir")),
        check_vma=False,
    )
```

```python
import jax
import jax.numpy as jnp
from jax import lax
from jax.sharding import PartitionSpec as P

STEPS = 4
BAND = 4


stencil_coef = (-205.0 / 72.0, 8.0 / 5.0, -1.0 / 5.0, 8.0 / 315.0, -1.0 / 560.0)


def laplace(padded_all, rows_here, depth, across):
    middle = padded_all[..., 4 : 4 + rows_here, 4 : 4 + depth, 4 : 4 + across]
    result = 3.0 * stencil_coef[0] * middle
    for reach in range(1, 5):
        plus_x = padded_all[..., 4 + reach : 4 + reach + rows_here, 4 : 4 + depth, 4 : 4 + across]
        minus_x = padded_all[..., 4 - reach : 4 - reach + rows_here, 4 : 4 + depth, 4 : 4 + across]
        plus_z = padded_all[..., 4 : 4 + rows_here, 4 + reach : 4 + reach + depth, 4 : 4 + across]
        minus_z = padded_all[..., 4 : 4 + rows_here, 4 - reach : 4 - reach + depth, 4 : 4 + across]
        plus_y = padded_all[..., 4 : 4 + rows_here, 4 : 4 + depth, 4 + reach : 4 + reach + across]
        minus_y = padded_all[..., 4 : 4 + rows_here, 4 : 4 + depth, 4 - reach : 4 - reach + across]
        result = result + stencil_coef[reach] * (
            plus_x + minus_x + plus_z + minus_z + plus_y + minus_y
        )
    return result


def band_matrix(owner, start, weight, n_tiles, n_rows):
    first = owner * n_rows + start
    place = jnp.arange(n_tiles * n_rows, dtype=jnp.int32)
    diff = place[None, None, :] - first[:, :, None]
    wide = weight.astype(jnp.bfloat16)
    zero = jnp.zeros((), jnp.bfloat16)
    out = jnp.where(diff == 0, wide[:, :, 0:1], zero)
    for k in range(1, BAND):
        out = jnp.where(diff == k, wide[:, :, k : k + 1], out)
    return out


def exchange_halo(tails, heads):
    count = lax.axis_size("tile")
    up = [(i, i + 1) for i in range(count - 1)]
    down = [(j, i) for i, j in up]
    return lax.ppermute(tails, "tile", up), lax.ppermute(heads, "tile", down)


def run_steps(field_now, field_old, speed_wide, rec_wide, snaps, rows_here):
    reach = 4
    halo = reach * STEPS
    _, _, depth, across = field_now.shape
    plane = lax.broadcasted_iota(jnp.int32, (1, 1, depth, 1), 2)
    image_sum = jnp.zeros((field_now.shape[0], rows_here, depth, across), jnp.float32)
    for step in range(STEPS):
        ext_in = halo - reach * step
        ext_out = ext_in - reach
        rows_out = rows_here + 2 * ext_out
        lo = (halo - reach) - ext_out
        padded_all = jnp.pad(field_now, ((0, 0), (0, 0), (4, 4), (4, 4)))
        curvature = laplace(padded_all, rows_out, depth, across)
        inject = rec_wide[step][:, lo : lo + rows_out, None, :]
        curvature = curvature + jnp.where(plane == 0, inject, 0.0)
        now_mid = field_now[:, reach : reach + rows_out]
        old_off = field_old.shape[1] // 2 - rows_out // 2
        old_mid = field_old[:, old_off : old_off + rows_out]
        speed_mid = speed_wide[:, lo : lo + rows_out]
        field_new = 2.0 * now_mid - old_mid + speed_mid * curvature
        image_sum = image_sum + snaps[step].astype(jnp.float32) * field_new[
            :, ext_out : ext_out + rows_here
        ]
        field_old, field_now = (field_now, field_new)
    return field_now, image_sum


def per_device(
    receiver_old, receiver_now, courant, source_snaps, recorded, row_owner, band_start, band_weight
):
    local_dirs, rows_here, depth, across = receiver_now.shape
    reach = 4
    halo = reach * STEPS
    old_halo = halo - reach
    traces = jnp.moveaxis(recorded, 0, 2)
    narrow_before, narrow_after = exchange_halo(
        jnp.concatenate([courant[:, -old_halo:], traces[:, -old_halo:]], axis=2),
        jnp.concatenate([courant[:, :old_halo], traces[:, :old_halo]], axis=2),
    )
    c_b, rec_b = narrow_before[:, :, :depth], jnp.moveaxis(narrow_before[:, :, depth:], 2, 0)
    c_a, rec_a = narrow_after[:, :, :depth], jnp.moveaxis(narrow_after[:, :, depth:], 2, 0)
    speed_all = jnp.concatenate([c_b, courant, c_a], axis=1).astype(jnp.float32)
    rec_all = jnp.concatenate([rec_b, recorded, rec_a], axis=2).astype(jnp.float32)
    fields = []
    images = []
    for d in range(local_dirs):
        now_d = receiver_now[d : d + 1]
        old_d = receiver_old[d : d + 1]
        wide_before, wide_after = exchange_halo(
            jnp.concatenate([now_d[:, -halo:], old_d[:, -old_halo:]], axis=1),
            jnp.concatenate([now_d[:, :halo], old_d[:, :old_halo]], axis=1),
        )
        if fields:
            fields[-1], images[-1], wide_before, wide_after = lax.optimization_barrier(
                (fields[-1], images[-1], wide_before, wide_after)
            )
        field_now = jnp.concatenate([wide_before[:, :halo], now_d, wide_after[:, :halo]], axis=1)
        field_old = jnp.concatenate([wide_before[:, halo:], old_d, wide_after[:, halo:]], axis=1)
        field_now, image_d = run_steps(
            field_now,
            field_old,
            speed_all[d : d + 1],
            rec_all[:, d : d + 1],
            source_snaps[:, d : d + 1],
            rows_here,
        )
        fields.append(field_now)
        images.append(image_d)
    field_now = jnp.concatenate(fields, axis=0)
    image_sum = jnp.concatenate(images, axis=0)
    image_flat = image_sum.astype(jnp.bfloat16).reshape(local_dirs, rows_here, depth * across)
    n_dir = lax.axis_size("dir")
    n_tiles = lax.axis_size("tile")
    cols = depth * across // n_dir
    blocks = image_flat.reshape(local_dirs, rows_here, n_dir, cols)
    got = lax.all_to_all(blocks, "dir", split_axis=2, concat_axis=0, tiled=True)
    all_dirs = got.shape[0]
    got = got.reshape(all_dirs * rows_here, cols)
    owner = row_owner[:, :, 0]
    mt = band_matrix(owner, band_start, band_weight, n_tiles, rows_here)
    mt = mt.reshape(all_dirs * rows_here, n_tiles * rows_here)
    partial = lax.dot_general(
        mt, got, (((0,), (0,)), ((), ())), preferred_element_type=jnp.float32
    )
    partial = partial.reshape(n_tiles, rows_here * cols)
    sent = lax.all_to_all(partial, "tile", split_axis=0, concat_axis=0, tiled=True)
    stack = jnp.sum(sent.reshape(n_tiles, rows_here, cols), axis=0)
    return (field_now, stack)


def solution(mesh):
    return jax.shard_map(
        per_device,
        mesh=mesh,
        in_specs=(
            P("dir", "tile", None, None),
            P("dir", "tile", None, None),
            P("dir", "tile", None, None),
            P(None, "dir", "tile", None, None),
            P(None, "dir", "tile", None),
            P(None, "tile", None),
            P(None, "tile"),
            P(None, "tile", None),
        ),
        out_specs=(P("dir", "tile", None, None), P("tile", "dir")),
        check_vma=False,
    )
```

```python
import jax
import jax.numpy as jnp
from jax import lax
from jax.sharding import PartitionSpec as P

STEPS = 4
BAND = 4


stencil_coef = (-205.0 / 72.0, 8.0 / 5.0, -1.0 / 5.0, 8.0 / 315.0, -1.0 / 560.0)


def laplace(padded_all, rows_here, depth, across):
    middle = padded_all[..., 4 : 4 + rows_here, 4 : 4 + depth, 4 : 4 + across]
    result = 3.0 * stencil_coef[0] * middle
    for reach in range(1, 5):
        plus_x = padded_all[..., 4 + reach : 4 + reach + rows_here, 4 : 4 + depth, 4 : 4 + across]
        minus_x = padded_all[..., 4 - reach : 4 - reach + rows_here, 4 : 4 + depth, 4 : 4 + across]
        plus_z = padded_all[..., 4 : 4 + rows_here, 4 + reach : 4 + reach + depth, 4 : 4 + across]
        minus_z = padded_all[..., 4 : 4 + rows_here, 4 - reach : 4 - reach + depth, 4 : 4 + across]
        plus_y = padded_all[..., 4 : 4 + rows_here, 4 : 4 + depth, 4 + reach : 4 + reach + across]
        minus_y = padded_all[..., 4 : 4 + rows_here, 4 : 4 + depth, 4 - reach : 4 - reach + across]
        result = result + stencil_coef[reach] * (
            plus_x + minus_x + plus_z + minus_z + plus_y + minus_y
        )
    return result


def band_matrix(owner, start, weight, n_tiles, n_rows):
    first = owner * n_rows + start
    place = jnp.arange(n_tiles * n_rows, dtype=jnp.int32)
    diff = place[None, None, :] - first[:, :, None]
    wide = weight.astype(jnp.bfloat16)
    zero = jnp.zeros((), jnp.bfloat16)
    out = jnp.where(diff == 0, wide[:, :, 0:1], zero)
    for k in range(1, BAND):
        out = jnp.where(diff == k, wide[:, :, k : k + 1], out)
    return out


def exchange_halo(tails, heads):
    count = lax.axis_size("tile")
    up = [(i, i + 1) for i in range(count - 1)]
    down = [(j, i) for i, j in up]
    return lax.ppermute(tails, "tile", up), lax.ppermute(heads, "tile", down)


def per_device(
    receiver_old, receiver_now, courant, source_snaps, recorded, row_owner, band_start, band_weight
):
    local_dirs, rows_here, depth, across = receiver_now.shape
    reach = 4
    halo = reach * STEPS
    old_halo = halo - reach
    wide_before, wide_after = exchange_halo(
        jnp.concatenate([receiver_now[:, -halo:], receiver_old[:, -old_halo:]], axis=1),
        jnp.concatenate([receiver_now[:, :halo], receiver_old[:, :old_halo]], axis=1),
    )
    traces = jnp.moveaxis(recorded[: STEPS - 1], 0, 2)
    narrow_before, narrow_after = exchange_halo(
        jnp.concatenate([courant[:, -old_halo:], traces[:, -old_halo:]], axis=2),
        jnp.concatenate([courant[:, :old_halo], traces[:, :old_halo]], axis=2),
    )
    now_b, old_b = wide_before[:, :halo], wide_before[:, halo:]
    now_a, old_a = wide_after[:, :halo], wide_after[:, halo:]
    unread = jnp.zeros((1, local_dirs, old_halo, across), recorded.dtype)
    c_b = narrow_before[:, :, :depth]
    c_a = narrow_after[:, :, :depth]
    rec_b = jnp.concatenate([jnp.moveaxis(narrow_before[:, :, depth:], 2, 0), unread], axis=0)
    rec_a = jnp.concatenate([jnp.moveaxis(narrow_after[:, :, depth:], 2, 0), unread], axis=0)
    field_now = jnp.concatenate([now_b, receiver_now, now_a], axis=1)
    field_old = jnp.concatenate([old_b, receiver_old, old_a], axis=1)
    speed_wide = jnp.concatenate([c_b, courant, c_a], axis=1).astype(jnp.float32)
    rec_wide = jnp.concatenate([rec_b, recorded, rec_a], axis=2).astype(jnp.float32)
    plane = lax.broadcasted_iota(jnp.int32, (1, 1, depth, 1), 2)
    image_sum = jnp.zeros(receiver_now.shape, jnp.float32)
    for step in range(STEPS):
        ext_in = halo - reach * step
        ext_out = ext_in - reach
        rows_out = rows_here + 2 * ext_out
        lo = (halo - reach) - ext_out
        padded_all = jnp.pad(field_now, ((0, 0), (0, 0), (4, 4), (4, 4)))
        curvature = laplace(padded_all, rows_out, depth, across)
        inject = rec_wide[step][:, lo : lo + rows_out, None, :]
        curvature = curvature + jnp.where(plane == 0, inject, 0.0)
        now_mid = field_now[:, reach : reach + rows_out]
        old_off = field_old.shape[1] // 2 - rows_out // 2
        old_mid = field_old[:, old_off : old_off + rows_out]
        speed_mid = speed_wide[:, lo : lo + rows_out]
        field_new = 2.0 * now_mid - old_mid + speed_mid * curvature
        image_sum = image_sum + source_snaps[step].astype(jnp.float32) * field_new[
            :, ext_out : ext_out + rows_here
        ]
        field_old, field_now = (field_now, field_new)
    image_flat = image_sum.astype(jnp.bfloat16).reshape(local_dirs, rows_here, depth * across)
    n_dir = lax.axis_size("dir")
    n_tiles = lax.axis_size("tile")
    cols = depth * across // n_dir
    blocks = image_flat.reshape(local_dirs, rows_here, n_dir, cols)
    got = lax.all_to_all(blocks, "dir", split_axis=2, concat_axis=0, tiled=True)
    all_dirs = got.shape[0]
    got = got.reshape(all_dirs * rows_here, cols)
    owner = row_owner[:, :, 0]
    mt = band_matrix(owner, band_start, band_weight, n_tiles, rows_here)
    mt = mt.reshape(all_dirs * rows_here, n_tiles * rows_here)
    partial = lax.dot_general(
        mt, got, (((0,), (0,)), ((), ())), preferred_element_type=jnp.float32
    )
    partial = partial.reshape(n_tiles, rows_here * cols)
    sent = lax.all_to_all(partial, "tile", split_axis=0, concat_axis=0, tiled=True)
    stack = jnp.sum(sent.reshape(n_tiles, rows_here, cols), axis=0)
    return (field_now, stack)


def solution(mesh):
    return jax.shard_map(
        per_device,
        mesh=mesh,
        in_specs=(
            P("dir", "tile", None, None),
            P("dir", "tile", None, None),
            P("dir", "tile", None, None),
            P(None, "dir", "tile", None, None),
            P(None, "dir", "tile", None),
            P(None, "tile", None),
            P(None, "tile"),
            P(None, "tile", None),
        ),
        out_specs=(P("dir", "tile", None, None), P("tile", "dir")),
        check_vma=False,
    )
```

```python
import jax
import jax.numpy as jnp
from jax import lax
from jax.sharding import PartitionSpec as P

STEPS = 4
BAND = 4


stencil_coef = (-205.0 / 72.0, 8.0 / 5.0, -1.0 / 5.0, 8.0 / 315.0, -1.0 / 560.0)


def laplace(padded_all, rows_here, depth, across):
    middle = padded_all[..., 4 : 4 + rows_here, 4 : 4 + depth, 4 : 4 + across]
    result = 3.0 * stencil_coef[0] * middle
    for reach in range(1, 5):
        plus_x = padded_all[..., 4 + reach : 4 + reach + rows_here, 4 : 4 + depth, 4 : 4 + across]
        minus_x = padded_all[..., 4 - reach : 4 - reach + rows_here, 4 : 4 + depth, 4 : 4 + across]
        plus_z = padded_all[..., 4 : 4 + rows_here, 4 + reach : 4 + reach + depth, 4 : 4 + across]
        minus_z = padded_all[..., 4 : 4 + rows_here, 4 - reach : 4 - reach + depth, 4 : 4 + across]
        plus_y = padded_all[..., 4 : 4 + rows_here, 4 : 4 + depth, 4 + reach : 4 + reach + across]
        minus_y = padded_all[..., 4 : 4 + rows_here, 4 : 4 + depth, 4 - reach : 4 - reach + across]
        result = result + stencil_coef[reach] * (
            plus_x + minus_x + plus_z + minus_z + plus_y + minus_y
        )
    return result


def band_matrix(owner, start, weight, n_tiles, n_rows):
    first = owner * n_rows + start
    place = jnp.arange(n_tiles * n_rows, dtype=jnp.int32)
    diff = place[None, None, :] - first[:, :, None]
    wide = weight.astype(jnp.bfloat16)
    zero = jnp.zeros((), jnp.bfloat16)
    out = jnp.where(diff == 0, wide[:, :, 0:1], zero)
    for k in range(1, BAND):
        out = jnp.where(diff == k, wide[:, :, k : k + 1], out)
    return out


def exchange_halo(tails, heads):
    count = lax.axis_size("tile")
    up = [(i, i + 1) for i in range(count - 1)]
    down = [(j, i) for i, j in up]
    return lax.ppermute(tails, "tile", up), lax.ppermute(heads, "tile", down)


def per_device(
    receiver_old, receiver_now, courant, source_snaps, recorded, row_owner, band_start, band_weight
):
    local_dirs, rows_here, depth, across = receiver_now.shape
    reach = 4
    halo = reach * STEPS
    old_halo = halo - reach
    wide_before, wide_after = exchange_halo(
        jnp.concatenate([receiver_now[:, -halo:], receiver_old[:, -old_halo:]], axis=1),
        jnp.concatenate([receiver_now[:, :halo], receiver_old[:, :old_halo]], axis=1),
    )
    traces = jnp.moveaxis(recorded[: STEPS - 1], 0, 2)
    narrow_before, narrow_after = exchange_halo(
        jnp.concatenate([courant[:, -old_halo:], traces[:, -old_halo:]], axis=2),
        jnp.concatenate([courant[:, :old_halo], traces[:, :old_halo]], axis=2),
    )
    now_b, old_b = wide_before[:, :halo], wide_before[:, halo:]
    now_a, old_a = wide_after[:, :halo], wide_after[:, halo:]
    unread = jnp.zeros((1, local_dirs, old_halo, across), recorded.dtype)
    c_b = narrow_before[:, :, :depth]
    c_a = narrow_after[:, :, :depth]
    rec_b = jnp.concatenate([jnp.moveaxis(narrow_before[:, :, depth:], 2, 0), unread], axis=0)
    rec_a = jnp.concatenate([jnp.moveaxis(narrow_after[:, :, depth:], 2, 0), unread], axis=0)
    field_now = jnp.concatenate([now_b, receiver_now, now_a], axis=1)
    field_old = jnp.concatenate([old_b, receiver_old, old_a], axis=1)
    speed_wide = jnp.concatenate([c_b, courant, c_a], axis=1).astype(jnp.float32)
    rec_wide = jnp.concatenate([rec_b, recorded, rec_a], axis=2).astype(jnp.float32)
    plane = lax.broadcasted_iota(jnp.int32, (1, 1, depth, 1), 2)
    image_sum = jnp.zeros(receiver_now.shape, jnp.float32)
    for step in range(STEPS):
        ext_in = halo - reach * step
        ext_out = ext_in - reach
        rows_out = rows_here + 2 * ext_out
        lo = (halo - reach) - ext_out
        padded_all = jnp.pad(field_now, ((0, 0), (0, 0), (4, 4), (4, 4)))
        curvature = laplace(padded_all, rows_out, depth, across)
        inject = rec_wide[step][:, lo : lo + rows_out, None, :]
        curvature = curvature + jnp.where(plane == 0, inject, 0.0)
        now_mid = field_now[:, reach : reach + rows_out]
        old_off = field_old.shape[1] // 2 - rows_out // 2
        old_mid = field_old[:, old_off : old_off + rows_out]
        speed_mid = speed_wide[:, lo : lo + rows_out]
        field_new = 2.0 * now_mid - old_mid + speed_mid * curvature
        image_sum = image_sum + source_snaps[step].astype(jnp.float32) * field_new[
            :, ext_out : ext_out + rows_here
        ]
        field_old, field_now = (field_now, field_new)
    image_flat = image_sum.astype(jnp.bfloat16).reshape(local_dirs, rows_here, depth * across)
    n_dir = lax.axis_size("dir")
    n_tiles = lax.axis_size("tile")
    cols = depth * across // n_dir
    blocks = image_flat.reshape(local_dirs, rows_here, n_dir, cols)
    got = lax.all_to_all(blocks, "dir", split_axis=2, concat_axis=0, tiled=True)
    all_dirs = got.shape[0]
    got = got.reshape(all_dirs * rows_here, cols)
    owner = row_owner[:, :, 0]
    capacity = max(2, 2 * rows_here // n_tiles)
    hits = (owner[:, :, None] == jnp.arange(n_tiles, dtype=jnp.int32)[None, None, :]).astype(jnp.int32)
    rank = jnp.sum((jnp.cumsum(hits, axis=1) - hits) * hits, axis=2)
    slot = owner * capacity + rank
    select = (
        slot[:, None, :] == jnp.arange(n_tiles * capacity, dtype=jnp.int32)[None, :, None]
    ).astype(jnp.bfloat16)
    diff = jnp.arange(rows_here, dtype=jnp.int32)[None, None, :] - band_start[:, :, None]
    wide = band_weight.astype(jnp.bfloat16)
    band = jnp.where(diff == 0, wide[:, :, 0:1], jnp.zeros((), jnp.bfloat16))
    for k in range(1, BAND):
        band = jnp.where(diff == k, wide[:, :, k : k + 1], band)
    got = got.reshape(all_dirs, rows_here, cols)
    slot_rows = jnp.einsum("dsr,drc->dsc", select, got, preferred_element_type=jnp.float32)
    slot_band = jnp.einsum("dsr,drj->dsj", select, band, preferred_element_type=jnp.float32)
    slot_rows = slot_rows.astype(jnp.bfloat16).reshape(all_dirs, n_tiles, capacity, cols)
    slot_band = slot_band.astype(jnp.bfloat16).reshape(all_dirs, n_tiles, capacity, rows_here)
    partial = jnp.einsum(
        "doqj,doqc->ojc", slot_band, slot_rows, preferred_element_type=jnp.float32
    )
    partial = partial.reshape(n_tiles, rows_here * cols)
    sent = lax.all_to_all(partial, "tile", split_axis=0, concat_axis=0, tiled=True)
    stack = jnp.sum(sent.reshape(n_tiles, rows_here, cols), axis=0)
    return (field_now, stack)


def solution(mesh):
    return jax.shard_map(
        per_device,
        mesh=mesh,
        in_specs=(
            P("dir", "tile", None, None),
            P("dir", "tile", None, None),
            P("dir", "tile", None, None),
            P(None, "dir", "tile", None, None),
            P(None, "dir", "tile", None),
            P(None, "tile", None),
            P(None, "tile"),
            P(None, "tile", None),
        ),
        out_specs=(P("dir", "tile", None, None), P("tile", "dir")),
        check_vma=False,
    )
```
